256 devices in a mesh: tm: 64 (over z, x, core), wafer: 4 (over y).
Axes of the slice: x: 4, y: 4, z: 8, core: 2. Of those that a mesh axis runs over, the one named last changes fastest.
Arguments:
- timestream: bfloat16 [1024, 262144], P('wafer', 'tm'), may hold values from -6 to 6
- sample_weight: bfloat16 [1024, 262144], P('wafer', 'tm'), may hold values from 0 to 4
- response: float32 [3, 1024], replicated, may hold values from -1 to 1
- band_filter: bfloat16 [256, 256], replicated, may hold values from -0.375 to 0.375
- whiten: bfloat16 [7, 1024, 1024], P(None, ('tm', 'wafer')), as said below
- group_wafer: int32 [64], replicated, may hold values from 0 to 6
- pointing: bfloat16 [1024, 6, 256, 256], P(('tm', 'wafer')), may hold values from -0.15625 to 0.15625
- tile_list: int32 [1024, 6], P(('tm', 'wafer')), may hold values from 0 to 2047, as said below
- tile_home: int32 [2048], replicated, may hold values from 0 to 2047, as said below
- solution: float32 [2048, 3, 256], P('tm'), may hold values from -6 to 6
- direction: float32 [2048, 3, 256], P('tm'), may hold values from -6 to 6
- cg_scalars: float32 [2], replicated, may hold values from 0.5 to 1.5
Outputs:
- solution_next: float32 [2048, 3, 256], P('tm')
- residual_next: float32 [2048, 3, 256], P('tm')
- direction_next: float32 [2048, 3, 256], P('tm')
The draws below stay inside these ranges and needn't reach their ends.
Inputs may be any that keep to these rules, and one draw needn't show every extreme that they name: `tile_list`: the tiles named in the spans of one device (one index of tm and one of wafer) are all different; among them at most 2 have their row tile_home on one index of tm, and in every draw, for each index of wafer, some index of tm owns exactly 2 tiles named by every device of that wafer index. A permutation: row tile_home[i] of a map holds sky tile i. `whiten`: each whitening matrix is symmetric.
All inputs are finite; a program needn't handle non-finite values.
Results may differ from the reference program's by a relative error of at most 0.0033.
The reference program's roundings to bfloat16 on the way (of `short_map`, `errors`, `filtered`, `whitened`, `smoothed` and `stokes`) count: a program that leaves them out, or rounds other values in their place, can miss the bound.
Values may be sent and summed in bfloat16 or wider, within the bound.
No kernel may reach another device: no remote copies, remote signals or barrier semaphores. Data moves between devices by JAX's collectives and lax.ppermute only.
A program may use at most 128 MiB of HBM per device.

```python
import math
import jax
import jax.numpy as jnp
from jax import lax

WDET = 1024
WAFERS = 7
NSAMP = 256
NPIX = 256
NCOMP = 3
HITS = 6
TILE_DEV = 32
SPAN_GRP = 16
SPANS = 1024
NTILES = 2048
ROWS = 24
CAP = 2
N_TM = 64
N_WAFER = 4


def home_table(key):
    return jax.random.permutation(jax.random.fold_in(key, 7), NTILES).astype(jnp.int32)


def draw_tile_home(key, part):
    return home_table(key)


def draw_tile_list(key, part):
    home_slots = home_table(key)
    inverse = jnp.argsort(home_slots).astype(jnp.int32)
    device_count = N_TM * N_WAFER
    slot_count = N_TM * CAP
    key_score = jax.random.fold_in(key, 21)
    key_full = jax.random.fold_in(key, 22)
    key_base = jax.random.fold_in(key, 23)
    key_shuffle = jax.random.fold_in(key, 24)
    positions = jnp.arange(slot_count, dtype=jnp.int32)
    scores = jax.random.randint(key_score, (device_count, slot_count), 0, 1 << 20) * slot_count + positions[None, :]
    full_owner = jax.random.randint(key_full, (N_WAFER,), 0, N_TM)
    device_full = full_owner[jnp.arange(device_count, dtype=jnp.int32) % N_WAFER]
    forced = (positions // CAP)[None, :] == device_full[:, None]
    scores = jnp.where(forced, scores - (1 << 28), scores)
    picked = jnp.argsort(scores, axis=1)[:, :ROWS].astype(jnp.int32)
    row_index = jnp.arange(ROWS, dtype=jnp.int32)
    shuffle_scores = jax.random.randint(key_shuffle, (device_count, ROWS), 0, 1 << 20) * ROWS + row_index[None, :]
    shuffle_order = jnp.argsort(shuffle_scores, axis=1)
    picked = jnp.take_along_axis(picked, shuffle_order, axis=1)
    owner_pick = picked // CAP
    rank_pick = picked % CAP
    base_slot = jax.random.randint(key_base, (device_count, N_TM), 0, TILE_DEV)
    base_pick = jnp.take_along_axis(base_slot, owner_pick, axis=1)
    local_slot = (base_pick + rank_pick) % TILE_DEV
    slot_rows = owner_pick * TILE_DEV + local_slot
    tile_ids = jnp.take(inverse, slot_rows.reshape(-1), axis=0)
    return tile_ids.reshape(SPANS, HITS).astype(jnp.int32)


def draw_whiten(key, part):
    key_off = jax.random.fold_in(key, 3)
    key_diag = jax.random.fold_in(key, 4)
    spread = 0.35
    lower_end = 0.75
    upper_end = 1.25
    uniform_part = jax.random.uniform(key_off, (WAFERS, WDET, WDET), jnp.float32, -1.0, 1.0)
    symmetric = (uniform_part + jnp.swapaxes(uniform_part, 1, 2)) * (spread / math.sqrt(WDET))
    diagonal = jax.random.uniform(key_diag, (WAFERS, WDET), jnp.float32, lower_end, upper_end)
    identity = jnp.eye(WDET, dtype=jnp.float32)
    return (symmetric * (1.0 - identity)[None, :, :] + identity[None, :, :] * diagonal[:, None, :]).astype(jnp.bfloat16)


def draw_sample_weight(key, part):
    run_count = SPANS * NSAMP // 16
    key_level = jax.random.fold_in(key, 41)
    key_jitter = jax.random.fold_in(key, 42)
    key_cut = jax.random.fold_in(key, 43)
    level = jax.random.uniform(key_level, (WDET, 1, 1), jnp.float32, 0.5, 2.0)
    jitter = jax.random.uniform(key_jitter, (WDET, run_count, 16), jnp.float32, 0.6, 1.4)
    kept = (jax.random.randint(key_cut, (WDET, run_count, 1), 0, 8) != 0).astype(jnp.float32)
    return (level * jitter * kept).reshape(WDET, SPANS * NSAMP).astype(jnp.bfloat16)


def with_ends(result, own_key, low, high):
    longest = result.shape.index(max(result.shape))
    spots = []
    for shift in (0, 1):
        where = [jax.random.randint(jax.random.fold_in(own_key, axis), (), 0, length) for axis, length in enumerate(result.shape)]
        where[longest] = (where[longest] + shift) % result.shape[longest]
        spots.append(tuple(where))
    return result.at[spots[0]].set(low).at[spots[1]].set(high)


def shard_levels(stream_key, shape, cuts, least, high):
    loudness, own = 1.0, jax.random.fold_in(stream_key, 6)
    for axis_at, blocks in cuts:
        steps = jnp.exp(jax.random.uniform(jax.random.fold_in(own, axis_at), (blocks,), jnp.float32, least / len(cuts), high / len(cuts)))
        loudness = loudness * jnp.repeat(steps, shape[axis_at] // blocks).reshape([-1 if axis == axis_at else 1 for axis in range(len(shape))])
    return loudness


def gaussian(key, extent, scale, bound, split=(), kind=jnp.bfloat16):
    drawn = jax.random.normal(key, extent, jnp.float32) * scale
    if len(split) > 0:
        drawn = shard_levels(key, extent, split, -0.22, 0.18) * drawn
    return jnp.clip(drawn, min=-bound, max=bound).astype(kind)


def setup_inputs(seed: int = 0) -> dict:
    keys = jax.random.split(jax.random.key(seed), 13)
    timestream = gaussian(keys[0], (WDET, SPANS * NSAMP), 1.0, 6.0, ((0, 4), (1, 64)))
    sample_weight = draw_sample_weight(jax.random.fold_in(keys[12], 71), 0)
    response = jnp.clip(jax.random.uniform(keys[2], (NCOMP, WDET), jnp.float32, -1.0, 1.0), -1.0, 1.0)
    band_filter = gaussian(keys[3], (NSAMP, NSAMP), NSAMP ** -0.5, 0.375)
    whiten = draw_whiten(jax.random.fold_in(keys[12], 71), 0)
    group_wafer = with_ends(jax.random.randint(keys[5], (N_TM,), 0, WAFERS), jax.random.fold_in(keys[5], 1), 0, WAFERS - 1).astype(jnp.int32)
    pointing = gaussian(keys[6], (SPANS, HITS, NSAMP, NPIX), (HITS * NPIX) ** -0.5, 0.15625, ((0, 256),))
    tile_list = draw_tile_list(jax.random.fold_in(keys[12], 71), 0)
    tile_home = draw_tile_home(jax.random.fold_in(keys[12], 71), 0)
    solution = gaussian(keys[9], (NTILES, NCOMP, NPIX), 1.0, 6.0, ((0, 64),), jnp.float32)
    direction = gaussian(keys[10], (NTILES, NCOMP, NPIX), 1.0, 6.0, ((0, 64),), jnp.float32)
    cg_scalars = jnp.clip(jax.random.uniform(keys[11], (2,), jnp.float32, 0.5, 1.5), 0.5, 1.5)
    return {"timestream": timestream, "sample_weight": sample_weight, "response": response, "band_filter": band_filter, "whiten": whiten, "group_wafer": group_wafer, "pointing": pointing, "tile_list": tile_list, "tile_home": tile_home, "solution": solution, "direction": direction, "cg_scalars": cg_scalars}


def reference(timestream, sample_weight, response, band_filter, whiten, group_wafer, pointing, tile_list, tile_home, solution, direction, cg_scalars):
    precise_mode = lax.Precision.HIGHEST
    step_size = cg_scalars[0]
    blend_weight = cg_scalars[1]
    updated = solution + step_size * direction
    short_map = updated.astype(jnp.bfloat16)
    home_rows = jnp.take(tile_home, tile_list, axis=0).astype(jnp.int32)
    group_width = SPAN_GRP * NSAMP

    def group_term(group_idx):
        group_idx = group_idx.astype(jnp.int32)
        first_span = (group_idx * SPAN_GRP).astype(jnp.int32)
        first_sample = (group_idx * group_width).astype(jnp.int32)
        samples_grp = lax.dynamic_slice_in_dim(timestream, first_sample, group_width, 1).astype(jnp.float32)
        samples_grp = samples_grp.reshape(WDET, SPAN_GRP, NSAMP)
        weight_grp = lax.dynamic_slice_in_dim(sample_weight, first_sample, group_width, 1).astype(jnp.float32)
        weight_grp = weight_grp.reshape(WDET, SPAN_GRP, NSAMP)
        weights = lax.dynamic_slice_in_dim(pointing, first_span, SPAN_GRP, 0).astype(jnp.float32)
        rows_here = lax.dynamic_slice_in_dim(home_rows, first_span, SPAN_GRP, 0)
        tile_vals = jnp.take(short_map, rows_here, axis=0).astype(jnp.float32)
        signal_parts = jnp.einsum("cktp,ckjp->cjt", weights, tile_vals, precision=precise_mode)
        signal = jnp.einsum("jd,cjt->dct", response, signal_parts, precision=precise_mode)
        errors = ((samples_grp - signal) * weight_grp).astype(jnp.bfloat16)
        filtered = jnp.dot(errors.reshape(WDET * SPAN_GRP, NSAMP), band_filter, preferred_element_type=jnp.float32)
        filtered = filtered.astype(jnp.bfloat16).reshape(WDET, group_width)
        matrix = lax.dynamic_index_in_dim(whiten, group_wafer[group_idx], 0, keepdims=False)
        whitened = jnp.dot(matrix, filtered, preferred_element_type=jnp.float32).astype(jnp.bfloat16)
        smoothed = jnp.dot(whitened.reshape(WDET * SPAN_GRP, NSAMP), band_filter.T, preferred_element_type=jnp.float32)
        smoothed = smoothed.astype(jnp.bfloat16).reshape(WDET, SPAN_GRP, NSAMP)
        stokes = jnp.einsum("jd,dct->cjt", response, smoothed.astype(jnp.float32) * weight_grp, precision=precise_mode)
        stokes = stokes.astype(jnp.bfloat16)
        return jnp.einsum("cjt,cktp->ckjp", stokes.astype(jnp.float32), weights, precision=precise_mode)

    partials = lax.map(group_term, jnp.arange(N_TM, dtype=jnp.int32))
    summed = jax.ops.segment_sum(partials.reshape(SPANS * HITS, NCOMP, NPIX), home_rows.reshape(SPANS * HITS), num_segments=NTILES)
    residual_next = summed * (float(WDET) ** -0.5)
    direction_next = residual_next + blend_weight * direction
    return (updated, residual_next, direction_next)
```

```python
import jax
import jax.numpy as jnp
from jax import lax
from jax.sharding import PartitionSpec as P


def shards(
    timestream,
    sample_weight,
    response,
    band_filter,
    whiten,
    group_wafer,
    pointing,
    tile_list,
    tile_home,
    solution,
    direction,
    cg_scalars,
):
    precise_mode = lax.Precision.HIGHEST
    tm_count = lax.axis_size("tm")
    tm_index = lax.axis_index("tm")
    step_size = cg_scalars[0]
    blend_weight = cg_scalars[1]
    updated = solution + step_size * direction
    short_map = updated.astype(jnp.bfloat16)
    tiles_own, comp_count, pixel_count = solution.shape
    spans_here, per_span = tile_list.shape
    samples = band_filter.shape[0]
    det_total = whiten.shape[2]
    row_count = spans_here * per_span
    capacity = max(2, (row_count + tm_count - 1) // tm_count)
    tile_ids = tile_list.reshape(row_count)
    home_rows = jnp.take(tile_home, tile_ids, axis=0)
    owners = home_rows // tiles_own
    local_slot = home_rows % tiles_own
    positions = jnp.arange(row_count, dtype=jnp.int32)
    earlier = (owners[:, None] == owners[None, :]) & (positions[None, :] < positions[:, None])
    before_count = jnp.sum(earlier.astype(jnp.int32), axis=1)
    targets = owners * capacity + before_count
    placing = targets[:, None] == jnp.arange(tm_count * capacity, dtype=jnp.int32)[None, :]
    requests = jnp.sum(jnp.where(placing, local_slot[:, None], 0), axis=0)
    requests = requests.reshape(tm_count, capacity)
    asked_slots = lax.all_to_all(requests, "tm", split_axis=0, concat_axis=0, tiled=True)
    served = jnp.take(short_map, asked_slots, axis=0)
    replies, asked_slots = (
        lax.all_to_all(served, "tm", split_axis=0, concat_axis=0, tiled=True),
        asked_slots,
    )
    fetched = jnp.take(
        replies.reshape(tm_count * capacity, comp_count, pixel_count), targets, axis=0
    )
    fetched = fetched.reshape(spans_here, per_span, comp_count, pixel_count)
    signal_parts = jnp.einsum(
        "cktp,ckjp->cjt", pointing, fetched, preferred_element_type=jnp.float32
    )
    block_rows = lax.all_gather(whiten, "wafer", axis=1, tiled=True)
    sent_blocks = jnp.take(block_rows, group_wafer, axis=0)
    matrix = lax.all_to_all(sent_blocks, "tm", split_axis=0, concat_axis=0, tiled=True)
    matrix = matrix.reshape(det_total, det_total)
    columns, column_weights = (
        lax.all_to_all(timestream, "wafer", split_axis=1, concat_axis=0, tiled=True),
        lax.all_to_all(sample_weight, "wafer", split_axis=1, concat_axis=0, tiled=True),
    )
    column_weights = column_weights.astype(jnp.float32).reshape(det_total, spans_here, samples)
    signal = jnp.einsum("jd,cjt->dct", response, signal_parts, precision=precise_mode)
    errors = (
        (columns.astype(jnp.float32).reshape(det_total, spans_here, samples) - signal)
        * column_weights
    ).astype(jnp.bfloat16)
    filtered = jnp.dot(
        errors.reshape(det_total * spans_here, samples),
        band_filter,
        preferred_element_type=jnp.float32,
    )
    filtered = filtered.astype(jnp.bfloat16).reshape(det_total, spans_here * samples)
    whitened = jnp.dot(matrix, filtered, preferred_element_type=jnp.float32).astype(jnp.bfloat16)
    smoothed = lax.dot_general(
        whitened.reshape(det_total * spans_here, samples),
        band_filter,
        (((1,), (1,)), ((), ())),
        preferred_element_type=jnp.float32,
    )
    smoothed = smoothed.astype(jnp.bfloat16).reshape(det_total, spans_here, samples)
    stokes = jnp.einsum(
        "jd,dct->cjt",
        response,
        smoothed.astype(jnp.float32) * column_weights,
        precision=precise_mode,
    )
    stokes_short = stokes.astype(jnp.bfloat16)
    partial_value = jnp.einsum(
        "cjt,cktp->ckjp", stokes_short, pointing, preferred_element_type=jnp.float32
    )
    partial_value = partial_value.reshape(row_count, comp_count * pixel_count)
    outgoing = jnp.dot(placing.astype(jnp.float32).T, partial_value, precision=precise_mode)
    outgoing = outgoing.reshape(tm_count, capacity, comp_count, pixel_count)
    arrived = lax.all_to_all(outgoing, "tm", split_axis=0, concat_axis=0, tiled=True)
    slot_hits = (
        asked_slots.reshape(-1)[None, :] == jnp.arange(tiles_own, dtype=jnp.int32)[:, None]
    ).astype(jnp.float32)
    owned_sum = jnp.dot(
        slot_hits,
        arrived.reshape(tm_count * capacity, comp_count * pixel_count),
        precision=precise_mode,
    )
    owned_sum = owned_sum.reshape(tiles_own, comp_count, pixel_count)
    summed = lax.psum(owned_sum, "wafer")
    residual_next = summed * float(det_total) ** (-0.5)
    direction_next = residual_next + blend_weight * direction
    return (updated, residual_next, direction_next)


def solution(mesh):
    in_specs = (
        P("wafer", "tm"),
        P("wafer", "tm"),
        P(),
        P(),
        P(None, ("tm", "wafer"), None),
        P(),
        P(("tm", "wafer"), None, None, None),
        P(("tm", "wafer"), None),
        P(),
        P("tm", None, None),
        P("tm", None, None),
        P(),
    )
    out_specs = (P("tm", None, None), P("tm", None, None), P("tm", None, None))
    return jax.shard_map(shards, mesh=mesh, in_specs=in_specs, out_specs=out_specs, check_vma=False)
```

```python
import jax
import jax.numpy as jnp
from jax import lax
from jax.sharding import PartitionSpec as P


def wafer_gather(x, axis):
    spot = lax.axis_index("wafer")
    size = lax.axis_size("wafer")
    bit = 1
    while bit < size:
        other = lax.ppermute(x, "wafer", [(i, i ^ bit) for i in range(size)])
        low = (spot & bit) == 0
        x = jnp.where(low, jnp.concatenate([x, other], axis), jnp.concatenate([other, x], axis))
        bit *= 2
    return x


def wafer_sum(x):
    size = lax.axis_size("wafer")
    bit = 1
    while bit < size:
        x = x + lax.ppermute(x, "wafer", [(i, i ^ bit) for i in range(size)])
        bit *= 2
    return x


def shards(
    timestream,
    sample_weight,
    response,
    band_filter,
    whiten,
    group_wafer,
    pointing,
    tile_list,
    tile_home,
    solution,
    direction,
    cg_scalars,
):
    precise_mode = lax.Precision.HIGHEST
    tm_count = lax.axis_size("tm")
    tm_index = lax.axis_index("tm")
    step_size = cg_scalars[0]
    blend_weight = cg_scalars[1]
    updated = solution + step_size * direction
    short_map = updated.astype(jnp.bfloat16)
    tiles_own, comp_count, pixel_count = solution.shape
    spans_here, per_span = tile_list.shape
    samples = band_filter.shape[0]
    det_total = whiten.shape[2]
    row_count = spans_here * per_span
    capacity = max(2, (row_count + tm_count - 1) // tm_count)
    tile_ids = tile_list.reshape(row_count)
    home_rows = jnp.take(tile_home, tile_ids, axis=0)
    owners = home_rows // tiles_own
    local_slot = home_rows % tiles_own
    positions = jnp.arange(row_count, dtype=jnp.int32)
    earlier = (owners[:, None] == owners[None, :]) & (positions[None, :] < positions[:, None])
    before_count = jnp.sum(earlier.astype(jnp.int32), axis=1)
    targets = owners * capacity + before_count
    placing = targets[:, None] == jnp.arange(tm_count * capacity, dtype=jnp.int32)[None, :]
    requests = jnp.sum(jnp.where(placing, local_slot[:, None], 0), axis=0)
    requests = requests.reshape(tm_count, capacity)
    asked_slots = lax.all_to_all(requests, "tm", split_axis=0, concat_axis=0, tiled=True)
    served = jnp.take(short_map, asked_slots, axis=0)
    replies, asked_slots = (
        lax.all_to_all(served, "tm", split_axis=0, concat_axis=0, tiled=True),
        asked_slots,
    )
    fetched = jnp.take(
        replies.reshape(tm_count * capacity, comp_count, pixel_count), targets, axis=0
    )
    fetched = fetched.reshape(spans_here, per_span, comp_count, pixel_count)
    signal_parts = jnp.einsum(
        "cktp,ckjp->cjt", pointing, fetched, preferred_element_type=jnp.float32
    )
    block_rows = wafer_gather(whiten, 1)
    sent_blocks = jnp.take(block_rows, group_wafer, axis=0)
    matrix = lax.all_to_all(sent_blocks, "tm", split_axis=0, concat_axis=0, tiled=True)
    matrix = matrix.reshape(det_total, det_total)
    columns, column_weights = (
        lax.all_to_all(timestream, "wafer", split_axis=1, concat_axis=0, tiled=True),
        lax.all_to_all(sample_weight, "wafer", split_axis=1, concat_axis=0, tiled=True),
    )
    column_weights = column_weights.astype(jnp.float32).reshape(det_total, spans_here, samples)
    signal = jnp.einsum("jd,cjt->dct", response, signal_parts, precision=precise_mode)
    errors = (
        (columns.astype(jnp.float32).reshape(det_total, spans_here, samples) - signal)
        * column_weights
    ).astype(jnp.bfloat16)
    filtered = jnp.dot(
        errors.reshape(det_total * spans_here, samples),
        band_filter,
        preferred_element_type=jnp.float32,
    )
    filtered = filtered.astype(jnp.bfloat16).reshape(det_total, spans_here * samples)
    whitened = jnp.dot(matrix, filtered, preferred_element_type=jnp.float32).astype(jnp.bfloat16)
    smoothed = lax.dot_general(
        whitened.reshape(det_total * spans_here, samples),
        band_filter,
        (((1,), (1,)), ((), ())),
        preferred_element_type=jnp.float32,
    )
    smoothed = smoothed.astype(jnp.bfloat16).reshape(det_total, spans_here, samples)
    stokes = jnp.einsum(
        "jd,dct->cjt",
        response,
        smoothed.astype(jnp.float32) * column_weights,
        precision=precise_mode,
    )
    stokes_short = stokes.astype(jnp.bfloat16)
    partial_value = jnp.einsum(
        "cjt,cktp->ckjp", stokes_short, pointing, preferred_element_type=jnp.float32
    )
    partial_value = partial_value.reshape(row_count, comp_count * pixel_count)
    outgoing = jnp.dot(placing.astype(jnp.float32).T, partial_value, precision=precise_mode)
    outgoing = outgoing.reshape(tm_count, capacity, comp_count, pixel_count)
    arrived = lax.all_to_all(outgoing, "tm", split_axis=0, concat_axis=0, tiled=True)
    slot_hits = (
        asked_slots.reshape(-1)[None, :] == jnp.arange(tiles_own, dtype=jnp.int32)[:, None]
    ).astype(jnp.float32)
    owned_sum = jnp.dot(
        slot_hits,
        arrived.reshape(tm_count * capacity, comp_count * pixel_count),
        precision=precise_mode,
    )
    owned_sum = owned_sum.reshape(tiles_own, comp_count, pixel_count)
    summed = wafer_sum(owned_sum)
    residual_next = summed * float(det_total) ** (-0.5)
    direction_next = residual_next + blend_weight * direction
    return (updated, residual_next, direction_next)


def solution(mesh):
    in_specs = (
        P("wafer", "tm"),
        P("wafer", "tm"),
        P(),
        P(),
        P(None, ("tm", "wafer"), None),
        P(),
        P(("tm", "wafer"), None, None, None),
        P(("tm", "wafer"), None),
        P(),
        P("tm", None, None),
        P("tm", None, None),
        P(),
    )
    out_specs = (P("tm", None, None), P("tm", None, None), P("tm", None, None))
    return jax.shard_map(shards, mesh=mesh, in_specs=in_specs, out_specs=out_specs, check_vma=False)
```

```python
import jax
import jax.numpy as jnp
from jax import lax
from jax.sharding import PartitionSpec as P


def wafer_gather(x, axis):
    spot = lax.axis_index("wafer")
    size = lax.axis_size("wafer")
    bit = 1
    while bit < size:
        other = lax.ppermute(x, "wafer", [(i, i ^ bit) for i in range(size)])
        low = (spot & bit) == 0
        x = jnp.where(low, jnp.concatenate([x, other], axis), jnp.concatenate([other, x], axis))
        bit *= 2
    return x


def wafer_columns(x):
    spot = lax.axis_index("wafer")
    size = lax.axis_size("wafer")
    width = x.shape[1] // size
    pieces = [lax.dynamic_slice_in_dim(x, spot * width, width, 1)]
    for shift in range(1, size):
        target = (spot + shift) % size
        piece = lax.dynamic_slice_in_dim(x, target * width, width, 1)
        pieces.append(lax.ppermute(piece, "wafer", [(i, (i + shift) % size) for i in range(size)]))
    stacked = jnp.stack(pieces)
    order = (spot - jnp.arange(size, dtype=jnp.int32)) % size
    return jnp.take(stacked, order, axis=0).reshape(size * x.shape[0], width)


def wafer_sum(x):
    size = lax.axis_size("wafer")
    bit = 1
    while bit < size:
        x = x + lax.ppermute(x, "wafer", [(i, i ^ bit) for i in range(size)])
        bit *= 2
    return x


def shards(
    timestream,
    sample_weight,
    response,
    band_filter,
    whiten,
    group_wafer,
    pointing,
    tile_list,
    tile_home,
    solution,
    direction,
    cg_scalars,
):
    precise_mode = lax.Precision.HIGHEST
    tm_count = lax.axis_size("tm")
    tm_index = lax.axis_index("tm")
    step_size = cg_scalars[0]
    blend_weight = cg_scalars[1]
    updated = solution + step_size * direction
    short_map = updated.astype(jnp.bfloat16)
    tiles_own, comp_count, pixel_count = solution.shape
    spans_here, per_span = tile_list.shape
    samples = band_filter.shape[0]
    det_total = whiten.shape[2]
    row_count = spans_here * per_span
    capacity = max(2, (row_count + tm_count - 1) // tm_count)
    tile_ids = tile_list.reshape(row_count)
    home_rows = jnp.take(tile_home, tile_ids, axis=0)
    owners = home_rows // tiles_own
    local_slot = home_rows % tiles_own
    positions = jnp.arange(row_count, dtype=jnp.int32)
    earlier = (owners[:, None] == owners[None, :]) & (positions[None, :] < positions[:, None])
    before_count = jnp.sum(earlier.astype(jnp.int32), axis=1)
    targets = owners * capacity + before_count
    placing = targets[:, None] == jnp.arange(tm_count * capacity, dtype=jnp.int32)[None, :]
    requests = jnp.sum(jnp.where(placing, local_slot[:, None], 0), axis=0)
    requests = requests.reshape(tm_count, capacity)
    asked_slots = lax.all_to_all(requests, "tm", split_axis=0, concat_axis=0, tiled=True)
    served = jnp.take(short_map, asked_slots, axis=0)
    replies, asked_slots = (
        lax.all_to_all(served, "tm", split_axis=0, concat_axis=0, tiled=True),
        asked_slots,
    )
    fetched = jnp.take(
        replies.reshape(tm_count * capacity, comp_count, pixel_count), targets, axis=0
    )
    fetched = fetched.reshape(spans_here, per_span, comp_count, pixel_count)
    signal_parts = jnp.einsum(
        "cktp,ckjp->cjt", pointing, fetched, preferred_element_type=jnp.float32
    )
    block_rows = wafer_gather(whiten, 1)
    sent_blocks = jnp.take(block_rows, group_wafer, axis=0)
    matrix = lax.all_to_all(sent_blocks, "tm", split_axis=0, concat_axis=0, tiled=True)
    matrix = matrix.reshape(det_total, det_total)
    columns = wafer_columns(timestream)
    column_weights = wafer_columns(sample_weight).astype(jnp.float32)
    width = spans_here * samples
    parts_flat = jnp.transpose(signal_parts, (1, 0, 2)).reshape(comp_count, width)
    signal = jnp.einsum("jd,js->ds", response, parts_flat, precision=precise_mode)
    errors = ((columns.astype(jnp.float32) - signal) * column_weights).astype(jnp.bfloat16)
    block_id = jnp.arange(width, dtype=jnp.int32) // samples
    same_span = block_id[:, None] == block_id[None, :]
    filter_blocks = jnp.where(same_span, jnp.tile(band_filter, (spans_here, spans_here)), jnp.zeros((), band_filter.dtype))
    filtered = jnp.dot(errors, filter_blocks, preferred_element_type=jnp.float32).astype(jnp.bfloat16)
    whitened = jnp.dot(matrix, filtered, preferred_element_type=jnp.float32).astype(jnp.bfloat16)
    smoothed = lax.dot_general(
        whitened, filter_blocks, (((1,), (1,)), ((), ())), preferred_element_type=jnp.float32
    ).astype(jnp.bfloat16)
    stokes = jnp.einsum(
        "jd,ds->js", response, smoothed.astype(jnp.float32) * column_weights, precision=precise_mode
    )
    stokes_short = jnp.transpose(stokes.reshape(comp_count, spans_here, samples), (1, 0, 2)).astype(jnp.bfloat16)
    partial_value = jnp.einsum(
        "cjt,cktp->ckjp", stokes_short, pointing, preferred_element_type=jnp.float32
    )
    partial_value = partial_value.reshape(row_count, comp_count * pixel_count)
    outgoing = jnp.dot(placing.astype(jnp.float32).T, partial_value, precision=precise_mode)
    outgoing = outgoing.reshape(tm_count, capacity, comp_count, pixel_count)
    arrived = lax.all_to_all(outgoing, "tm", split_axis=0, concat_axis=0, tiled=True)
    slot_hits = (
        asked_slots.reshape(-1)[None, :] == jnp.arange(tiles_own, dtype=jnp.int32)[:, None]
    ).astype(jnp.float32)
    owned_sum = jnp.dot(
        slot_hits,
        arrived.reshape(tm_count * capacity, comp_count * pixel_count),
        precision=precise_mode,
    )
    owned_sum = owned_sum.reshape(tiles_own, comp_count, pixel_count)
    summed = wafer_sum(owned_sum)
    residual_next = summed * float(det_total) ** (-0.5)
    direction_next = residual_next + blend_weight * direction
    return (updated, residual_next, direction_next)


def solution(mesh):
    in_specs = (
        P("wafer", "tm"),
        P("wafer", "tm"),
        P(),
        P(),
        P(None, ("tm", "wafer"), None),
        P(),
        P(("tm", "wafer"), None, None, None),
        P(("tm", "wafer"), None),
        P(),
        P("tm", None, None),
        P("tm", None, None),
        P(),
    )
    out_specs = (P("tm", None, None), P("tm", None, None), P("tm", None, None))
    return jax.shard_map(shards, mesh=mesh, in_specs=in_specs, out_specs=out_specs, check_vma=False)
```

```python
import jax
import jax.numpy as jnp
from jax import lax
from jax.sharding import PartitionSpec as P


def wafer_gather(x, axis):
    spot = lax.axis_index("wafer")
    size = lax.axis_size("wafer")
    bit = 1
    while bit < size:
        other = lax.ppermute(x, "wafer", [(i, i ^ bit) for i in range(size)])
        low = (spot & bit) == 0
        x = jnp.where(low, jnp.concatenate([x, other], axis), jnp.concatenate([other, x], axis))
        bit *= 2
    return x


def wafer_columns(x):
    spot = lax.axis_index("wafer")
    size = lax.axis_size("wafer")
    width = x.shape[1] // size
    pieces = [lax.dynamic_slice_in_dim(x, spot * width, width, 1)]
    for shift in range(1, size):
        target = (spot + shift) % size
        piece = lax.dynamic_slice_in_dim(x, target * width, width, 1)
        pieces.append(lax.ppermute(piece, "wafer", [(i, (i + shift) % size) for i in range(size)]))
    rows = x.shape[0]
    placed = jnp.zeros((size, rows, width), x.dtype)
    for shift, piece in enumerate(pieces):
        source = (spot - shift) % size
        placed = lax.dynamic_update_slice_in_dim(placed, piece[None], source, 0)
    return placed.reshape(size * rows, width)


def wafer_sum(x):
    size = lax.axis_size("wafer")
    bit = 1
    while bit < size:
        x = x + lax.ppermute(x, "wafer", [(i, i ^ bit) for i in range(size)])
        bit *= 2
    return x


def shards(
    timestream,
    sample_weight,
    response,
    band_filter,
    whiten,
    group_wafer,
    pointing,
    tile_list,
    tile_home,
    solution,
    direction,
    cg_scalars,
):
    precise_mode = lax.Precision.HIGHEST
    tm_count = lax.axis_size("tm")
    tm_index = lax.axis_index("tm")
    step_size = cg_scalars[0]
    blend_weight = cg_scalars[1]
    updated = solution + step_size * direction
    short_map = updated.astype(jnp.bfloat16)
    tiles_own, comp_count, pixel_count = solution.shape
    spans_here, per_span = tile_list.shape
    samples = band_filter.shape[0]
    det_total = whiten.shape[2]
    row_count = spans_here * per_span
    capacity = max(2, (row_count + tm_count - 1) // tm_count)
    tile_ids = tile_list.reshape(row_count)
    home_rows = jnp.take(tile_home, tile_ids, axis=0)
    owners = home_rows // tiles_own
    local_slot = home_rows % tiles_own
    positions = jnp.arange(row_count, dtype=jnp.int32)
    earlier = (owners[:, None] == owners[None, :]) & (positions[None, :] < positions[:, None])
    before_count = jnp.sum(earlier.astype(jnp.int32), axis=1)
    targets = owners * capacity + before_count
    placing = targets[:, None] == jnp.arange(tm_count * capacity, dtype=jnp.int32)[None, :]
    requests = jnp.sum(jnp.where(placing, local_slot[:, None], 0), axis=0)
    requests = requests.reshape(tm_count, capacity)
    asked_slots = lax.all_to_all(requests, "tm", split_axis=0, concat_axis=0, tiled=True)
    served = jnp.take(short_map, asked_slots, axis=0)
    replies, asked_slots = (
        lax.all_to_all(served, "tm", split_axis=0, concat_axis=0, tiled=True),
        asked_slots,
    )
    fetched = jnp.take(
        replies.reshape(tm_count * capacity, comp_count, pixel_count), targets, axis=0
    )
    fetched = fetched.reshape(spans_here, per_span, comp_count, pixel_count)
    signal_parts = jnp.einsum(
        "cktp,ckjp->cjt", pointing, fetched, preferred_element_type=jnp.float32
    )
    block_rows = wafer_gather(whiten, 1)
    sent_blocks = jnp.take(block_rows, group_wafer, axis=0)
    matrix = lax.all_to_all(sent_blocks, "tm", split_axis=0, concat_axis=0, tiled=True)
    matrix = matrix.reshape(det_total, det_total)
    columns = wafer_columns(timestream)
    column_weights = wafer_columns(sample_weight).astype(jnp.float32)
    width = spans_here * samples
    parts_flat = jnp.transpose(signal_parts, (1, 0, 2)).reshape(comp_count, width)
    signal = sum(response[j][:, None] * parts_flat[j][None, :] for j in range(comp_count))
    errors = ((columns.astype(jnp.float32) - signal) * column_weights).astype(jnp.bfloat16)
    block_id = jnp.arange(width, dtype=jnp.int32) // samples
    same_span = block_id[:, None] == block_id[None, :]
    filter_blocks = jnp.where(same_span, jnp.tile(band_filter, (spans_here, spans_here)), jnp.zeros((), band_filter.dtype))
    filtered = jnp.dot(errors, filter_blocks, preferred_element_type=jnp.float32).astype(jnp.bfloat16)
    whitened = jnp.dot(matrix, filtered, preferred_element_type=jnp.float32).astype(jnp.bfloat16)
    smoothed = lax.dot_general(
        whitened, filter_blocks, (((1,), (1,)), ((), ())), preferred_element_type=jnp.float32
    ).astype(jnp.bfloat16)
    weighted = smoothed.astype(jnp.float32) * column_weights
    stokes = jnp.stack([jnp.sum(response[j][:, None] * weighted, axis=0) for j in range(comp_count)])
    stokes_short = jnp.transpose(stokes.reshape(comp_count, spans_here, samples), (1, 0, 2)).astype(jnp.bfloat16)
    partial_value = jnp.einsum(
        "cjt,cktp->ckjp", stokes_short, pointing, preferred_element_type=jnp.float32
    )
    partial_value = partial_value.reshape(row_count, comp_count * pixel_count)
    outgoing = jnp.dot(placing.astype(jnp.float32).T, partial_value, precision=precise_mode)
    outgoing = outgoing.reshape(tm_count, capacity, comp_count, pixel_count)
    arrived = lax.all_to_all(outgoing, "tm", split_axis=0, concat_axis=0, tiled=True)
    slot_hits = (
        asked_slots.reshape(-1)[None, :] == jnp.arange(tiles_own, dtype=jnp.int32)[:, None]
    ).astype(jnp.float32)
    owned_sum = jnp.dot(
        slot_hits,
        arrived.reshape(tm_count * capacity, comp_count * pixel_count),
        precision=precise_mode,
    )
    owned_sum = owned_sum.reshape(tiles_own, comp_count, pixel_count)
    summed = wafer_sum(owned_sum)
    residual_next = summed * float(det_total) ** (-0.5)
    direction_next = residual_next + blend_weight * direction
    return (updated, residual_next, direction_next)


def solution(mesh):
    in_specs = (
        P("wafer", "tm"),
        P("wafer", "tm"),
        P(),
        P(),
        P(None, ("tm", "wafer"), None),
        P(),
        P(("tm", "wafer"), None, None, None),
        P(("tm", "wafer"), None),
        P(),
        P("tm", None, None),
        P("tm", None, None),
        P(),
    )
    out_specs = (P("tm", None, None), P("tm", None, None), P("tm", None, None))
    return jax.shard_map(shards, mesh=mesh, in_specs=in_specs, out_specs=out_specs, check_vma=False)
```

```python
import jax
import jax.numpy as jnp
from jax import lax
from jax.sharding import PartitionSpec as P


def wafer_gather(x, axis):
    spot = lax.axis_index("wafer")
    size = lax.axis_size("wafer")
    bit = 1
    while bit < size:
        other = lax.ppermute(x, "wafer", [(i, i ^ bit) for i in range(size)])
        low = (spot & bit) == 0
        x = jnp.where(low, jnp.concatenate([x, other], axis), jnp.concatenate([other, x], axis))
        bit *= 2
    return x


def wafer_columns(x):
    spot = lax.axis_index("wafer")
    size = lax.axis_size("wafer")
    width = x.shape[1] // size
    pieces = [lax.dynamic_slice_in_dim(x, spot * width, width, 1)]
    for shift in range(1, size):
        target = (spot + shift) % size
        piece = lax.dynamic_slice_in_dim(x, target * width, width, 1)
        pieces.append(lax.ppermute(piece, "wafer", [(i, (i + shift) % size) for i in range(size)]))
    rows = x.shape[0]
    placed = jnp.zeros((size, rows, width), x.dtype)
    for shift, piece in enumerate(pieces):
        source = (spot - shift) % size
        placed = lax.dynamic_update_slice_in_dim(placed, piece[None], source, 0)
    return placed.reshape(size * rows, width)


def symmetric_gather(block_rows, group_wafer, tm_index, tm_count):
    _, rows, det_total = block_rows.shape
    groups = 8
    lanes = det_total // groups
    sent_groups = groups // 2 + 1
    home_group = tm_index // (tm_count // groups)
    rolled = jnp.roll(block_rows, -home_group * lanes, axis=2)[:, :, : sent_groups * lanes]
    sent = jnp.take(rolled, group_wafer, axis=0)
    got = lax.all_to_all(sent, "tm", split_axis=0, concat_axis=0, tiled=True)
    got = got.reshape(groups, det_total // groups, sent_groups, lanes)
    band = []
    for g in range(groups):
        row = []
        for h in range(groups):
            d = (h - g) % groups
            if d < sent_groups:
                row.append(got[g, :, d, :])
            else:
                row.append(got[h, :, (g - h) % groups, :].T)
        band.append(jnp.concatenate(row, axis=1))
    return jnp.concatenate(band, axis=0)


def wafer_sum(x):
    size = lax.axis_size("wafer")
    bit = 1
    while bit < size:
        x = x + lax.ppermute(x, "wafer", [(i, i ^ bit) for i in range(size)])
        bit *= 2
    return x


def shards(
    timestream,
    sample_weight,
    response,
    band_filter,
    whiten,
    group_wafer,
    pointing,
    tile_list,
    tile_home,
    solution,
    direction,
    cg_scalars,
):
    precise_mode = lax.Precision.HIGHEST
    tm_count = lax.axis_size("tm")
    tm_index = lax.axis_index("tm")
    step_size = cg_scalars[0]
    blend_weight = cg_scalars[1]
    updated = solution + step_size * direction
    short_map = updated.astype(jnp.bfloat16)
    tiles_own, comp_count, pixel_count = solution.shape
    spans_here, per_span = tile_list.shape
    samples = band_filter.shape[0]
    det_total = whiten.shape[2]
    row_count = spans_here * per_span
    capacity = max(2, (row_count + tm_count - 1) // tm_count)
    tile_ids = tile_list.reshape(row_count)
    home_rows = jnp.take(tile_home, tile_ids, axis=0)
    owners = home_rows // tiles_own
    local_slot = home_rows % tiles_own
    positions = jnp.arange(row_count, dtype=jnp.int32)
    earlier = (owners[:, None] == owners[None, :]) & (positions[None, :] < positions[:, None])
    before_count = jnp.sum(earlier.astype(jnp.int32), axis=1)
    targets = owners * capacity + before_count
    placing = targets[:, None] == jnp.arange(tm_count * capacity, dtype=jnp.int32)[None, :]
    requests = jnp.sum(jnp.where(placing, local_slot[:, None], 0), axis=0)
    requests = requests.reshape(tm_count, capacity)
    asked_slots = lax.all_to_all(requests, "tm", split_axis=0, concat_axis=0, tiled=True)
    served = jnp.take(short_map, asked_slots, axis=0)
    replies, asked_slots = (
        lax.all_to_all(served, "tm", split_axis=0, concat_axis=0, tiled=True),
        asked_slots,
    )
    fetched = jnp.take(
        replies.reshape(tm_count * capacity, comp_count, pixel_count), targets, axis=0
    )
    fetched = fetched.reshape(spans_here, per_span, comp_count, pixel_count)
    signal_parts = jnp.einsum(
        "cktp,ckjp->cjt", pointing, fetched, preferred_element_type=jnp.float32
    )
    block_rows = wafer_gather(whiten, 1)
    matrix = symmetric_gather(block_rows, group_wafer, tm_index, tm_count)
    columns = wafer_columns(timestream)
    column_weights = wafer_columns(sample_weight).astype(jnp.float32)
    width = spans_here * samples
    parts_flat = jnp.transpose(signal_parts, (1, 0, 2)).reshape(comp_count, width)
    signal = sum(response[j][:, None] * parts_flat[j][None, :] for j in range(comp_count))
    errors = ((columns.astype(jnp.float32) - signal) * column_weights).astype(jnp.bfloat16)
    block_id = jnp.arange(width, dtype=jnp.int32) // samples
    same_span = block_id[:, None] == block_id[None, :]
    filter_blocks = jnp.where(same_span, jnp.tile(band_filter, (spans_here, spans_here)), jnp.zeros((), band_filter.dtype))
    filtered = jnp.dot(errors, filter_blocks, preferred_element_type=jnp.float32).astype(jnp.bfloat16)
    whitened = jnp.dot(matrix, filtered, preferred_element_type=jnp.float32).astype(jnp.bfloat16)
    smoothed = lax.dot_general(
        whitened, filter_blocks, (((1,), (1,)), ((), ())), preferred_element_type=jnp.float32
    ).astype(jnp.bfloat16)
    weighted = smoothed.astype(jnp.float32) * column_weights
    stokes = jnp.stack([jnp.sum(response[j][:, None] * weighted, axis=0) for j in range(comp_count)])
    stokes_short = jnp.transpose(stokes.reshape(comp_count, spans_here, samples), (1, 0, 2)).astype(jnp.bfloat16)
    partial_value = jnp.einsum(
        "cjt,cktp->ckjp", stokes_short, pointing, preferred_element_type=jnp.float32
    )
    partial_value = partial_value.reshape(row_count, comp_count * pixel_count)
    outgoing = jnp.dot(placing.astype(jnp.float32).T, partial_value, precision=precise_mode)
    outgoing = outgoing.reshape(tm_count, capacity, comp_count, pixel_count)
    arrived = lax.all_to_all(outgoing, "tm", split_axis=0, concat_axis=0, tiled=True)
    slot_hits = (
        asked_slots.reshape(-1)[None, :] == jnp.arange(tiles_own, dtype=jnp.int32)[:, None]
    ).astype(jnp.float32)
    owned_sum = jnp.dot(
        slot_hits,
        arrived.reshape(tm_count * capacity, comp_count * pixel_count),
        precision=precise_mode,
    )
    owned_sum = owned_sum.reshape(tiles_own, comp_count, pixel_count)
    summed = wafer_sum(owned_sum)
    residual_next = summed * float(det_total) ** (-0.5)
    direction_next = residual_next + blend_weight * direction
    return (updated, residual_next, direction_next)


def solution(mesh):
    in_specs = (
        P("wafer", "tm"),
        P("wafer", "tm"),
        P(),
        P(),
        P(None, ("tm", "wafer"), None),
        P(),
        P(("tm", "wafer"), None, None, None),
        P(("tm", "wafer"), None),
        P(),
        P("tm", None, None),
        P("tm", None, None),
        P(),
    )
    out_specs = (P("tm", None, None), P("tm", None, None), P("tm", None, None))
    return jax.shard_map(shards, mesh=mesh, in_specs=in_specs, out_specs=out_specs, check_vma=False)
```

```python
import jax
import jax.numpy as jnp
from jax import lax
from jax.sharding import PartitionSpec as P


def wafer_gather(x, axis):
    spot = lax.axis_index("wafer")
    size = lax.axis_size("wafer")
    bit = 1
    while bit < size:
        other = lax.ppermute(x, "wafer", [(i, i ^ bit) for i in range(size)])
        low = (spot & bit) == 0
        x = jnp.where(low, jnp.concatenate([x, other], axis), jnp.concatenate([other, x], axis))
        bit *= 2
    return x


def wafer_columns(x):
    spot = lax.axis_index("wafer")
    size = lax.axis_size("wafer")
    width = x.shape[1] // size
    pieces = [lax.dynamic_slice_in_dim(x, spot * width, width, 1)]
    for shift in range(1, size):
        target = (spot + shift) % size
        piece = lax.dynamic_slice_in_dim(x, target * width, width, 1)
        pieces.append(lax.ppermute(piece, "wafer", [(i, (i + shift) % size) for i in range(size)]))
    rows = x.shape[0]
    placed = jnp.zeros((size, rows, width), x.dtype)
    for shift, piece in enumerate(pieces):
        source = (spot - shift) % size
        placed = lax.dynamic_update_slice_in_dim(placed, piece[None], source, 0)
    return placed.reshape(size * rows, width)


def symmetric_gather(block_rows, group_wafer, tm_index, tm_count):
    _, rows, det_total = block_rows.shape
    groups = 8
    lanes = det_total // groups
    sent_groups = groups // 2 + 1
    home_group = tm_index // (tm_count // groups)
    rolled = jnp.roll(block_rows, -home_group * lanes, axis=2)[:, :, : sent_groups * lanes]
    sent = jnp.take(rolled, group_wafer, axis=0)
    got = lax.all_to_all(sent, "tm", split_axis=0, concat_axis=0, tiled=True)
    got = got.reshape(groups, det_total // groups, sent_groups, lanes)
    padded = jnp.pad(got, ((0, 0), (0, 0), (0, groups - sent_groups), (0, 0)))
    direct = jnp.stack([jnp.roll(padded[g], g, axis=1) for g in range(groups)])
    direct = direct.reshape(det_total, det_total)
    group_of = jnp.arange(det_total, dtype=jnp.int32) // lanes
    use_direct = (group_of[None, :] - group_of[:, None]) % groups < sent_groups
    return jnp.where(use_direct, direct, direct.T)


def wafer_sum(x):
    size = lax.axis_size("wafer")
    bit = 1
    while bit < size:
        x = x + lax.ppermute(x, "wafer", [(i, i ^ bit) for i in range(size)])
        bit *= 2
    return x


def shards(
    timestream,
    sample_weight,
    response,
    band_filter,
    whiten,
    group_wafer,
    pointing,
    tile_list,
    tile_home,
    solution,
    direction,
    cg_scalars,
):
    precise_mode = lax.Precision.HIGHEST
    tm_count = lax.axis_size("tm")
    tm_index = lax.axis_index("tm")
    step_size = cg_scalars[0]
    blend_weight = cg_scalars[1]
    updated = solution + step_size * direction
    short_map = updated.astype(jnp.bfloat16)
    tiles_own, comp_count, pixel_count = solution.shape
    spans_here, per_span = tile_list.shape
    samples = band_filter.shape[0]
    det_total = whiten.shape[2]
    row_count = spans_here * per_span
    capacity = max(2, (row_count + tm_count - 1) // tm_count)
    tile_ids = tile_list.reshape(row_count)
    home_rows = jnp.take(tile_home, tile_ids, axis=0)
    owners = home_rows // tiles_own
    local_slot = home_rows % tiles_own
    positions = jnp.arange(row_count, dtype=jnp.int32)
    earlier = (owners[:, None] == owners[None, :]) & (positions[None, :] < positions[:, None])
    before_count = jnp.sum(earlier.astype(jnp.int32), axis=1)
    targets = owners * capacity + before_count
    placing = targets[:, None] == jnp.arange(tm_count * capacity, dtype=jnp.int32)[None, :]
    requests = jnp.sum(jnp.where(placing, local_slot[:, None], 0), axis=0)
    requests = requests.reshape(tm_count, capacity)
    asked_slots = lax.all_to_all(requests, "tm", split_axis=0, concat_axis=0, tiled=True)
    served = jnp.take(short_map, asked_slots, axis=0)
    replies, asked_slots = (
        lax.all_to_all(served, "tm", split_axis=0, concat_axis=0, tiled=True),
        asked_slots,
    )
    fetched = jnp.take(
        replies.reshape(tm_count * capacity, comp_count, pixel_count), targets, axis=0
    )
    fetched = fetched.reshape(spans_here, per_span, comp_count, pixel_count)
    signal_parts = jnp.einsum(
        "cktp,ckjp->cjt", pointing, fetched, preferred_element_type=jnp.float32
    )
    block_rows = wafer_gather(whiten, 1)
    matrix = symmetric_gather(block_rows, group_wafer, tm_index, tm_count)
    columns = wafer_columns(timestream)
    column_weights = wafer_columns(sample_weight).astype(jnp.float32)
    width = spans_here * samples
    parts_flat = jnp.transpose(signal_parts, (1, 0, 2)).reshape(comp_count, width)
    signal = sum(response[j][:, None] * parts_flat[j][None, :] for j in range(comp_count))
    errors = ((columns.astype(jnp.float32) - signal) * column_weights).astype(jnp.bfloat16)
    block_id = jnp.arange(width, dtype=jnp.int32) // samples
    same_span = block_id[:, None] == block_id[None, :]
    filter_blocks = jnp.where(same_span, jnp.tile(band_filter, (spans_here, spans_here)), jnp.zeros((), band_filter.dtype))
    filtered = jnp.dot(errors, filter_blocks, preferred_element_type=jnp.float32).astype(jnp.bfloat16)
    whitened = jnp.dot(matrix, filtered, preferred_element_type=jnp.float32).astype(jnp.bfloat16)
    smoothed = lax.dot_general(
        whitened, filter_blocks, (((1,), (1,)), ((), ())), preferred_element_type=jnp.float32
    ).astype(jnp.bfloat16)
    weighted = smoothed.astype(jnp.float32) * column_weights
    stokes = jnp.stack([jnp.sum(response[j][:, None] * weighted, axis=0) for j in range(comp_count)])
    stokes_short = jnp.transpose(stokes.reshape(comp_count, spans_here, samples), (1, 0, 2)).astype(jnp.bfloat16)
    partial_value = jnp.einsum(
        "cjt,cktp->ckjp", stokes_short, pointing, preferred_element_type=jnp.float32
    )
    partial_value = partial_value.reshape(row_count, comp_count * pixel_count)
    outgoing = jnp.dot(placing.astype(jnp.float32).T, partial_value, precision=precise_mode)
    outgoing = outgoing.reshape(tm_count, capacity, comp_count, pixel_count)
    arrived = lax.all_to_all(outgoing, "tm", split_axis=0, concat_axis=0, tiled=True)
    slot_hits = (
        asked_slots.reshape(-1)[None, :] == jnp.arange(tiles_own, dtype=jnp.int32)[:, None]
    ).astype(jnp.float32)
    owned_sum = jnp.dot(
        slot_hits,
        arrived.reshape(tm_count * capacity, comp_count * pixel_count),
        precision=precise_mode,
    )
    owned_sum = owned_sum.reshape(tiles_own, comp_count, pixel_count)
    summed = wafer_sum(owned_sum)
    residual_next = summed * float(det_total) ** (-0.5)
    direction_next = residual_next + blend_weight * direction
    return (updated, residual_next, direction_next)


def solution(mesh):
    in_specs = (
        P("wafer", "tm"),
        P("wafer", "tm"),
        P(),
        P(),
        P(None, ("tm", "wafer"), None),
        P(),
        P(("tm", "wafer"), None, None, None),
        P(("tm", "wafer"), None),
        P(),
        P("tm", None, None),
        P("tm", None, None),
        P(),
    )
    out_specs = (P("tm", None, None), P("tm", None, None), P("tm", None, None))
    return jax.shard_map(shards, mesh=mesh, in_specs=in_specs, out_specs=out_specs, check_vma=False)
```

```python
import jax
import jax.numpy as jnp
from jax import lax
from jax.sharding import PartitionSpec as P


def wafer_gather(x, axis):
    spot = lax.axis_index("wafer")
    size = lax.axis_size("wafer")
    bit = 1
    while bit < size:
        other = lax.ppermute(x, "wafer", [(i, i ^ bit) for i in range(size)])
        low = (spot & bit) == 0
        x = jnp.where(low, jnp.concatenate([x, other], axis), jnp.concatenate([other, x], axis))
        bit *= 2
    return x


def wafer_columns(x):
    spot = lax.axis_index("wafer")
    size = lax.axis_size("wafer")
    width = x.shape[1] // size
    pieces = [lax.dynamic_slice_in_dim(x, spot * width, width, 1)]
    for shift in range(1, size):
        target = (spot + shift) % size
        piece = lax.dynamic_slice_in_dim(x, target * width, width, 1)
        pieces.append(lax.ppermute(piece, "wafer", [(i, (i + shift) % size) for i in range(size)]))
    rows = x.shape[0]
    placed = jnp.zeros((size, rows, width), x.dtype)
    for shift, piece in enumerate(pieces):
        source = (spot - shift) % size
        placed = lax.dynamic_update_slice_in_dim(placed, piece[None], source, 0)
    return placed.reshape(size * rows, width)


def symmetric_gather(block_rows, group_wafer, tm_index, tm_count):
    _, _, det_total = block_rows.shape
    groups = 8
    lanes = det_total // groups
    sent_groups = groups // 2 + 1
    home_group = tm_index // (tm_count // groups)
    rolled = jnp.roll(block_rows, -home_group * lanes, axis=2)[:, :, : sent_groups * lanes]
    sent = jnp.take(rolled, group_wafer, axis=0)
    got = lax.all_to_all(sent, "tm", split_axis=0, concat_axis=0, tiled=True)
    got = got.reshape(groups, det_total // groups, sent_groups, lanes)
    padded = jnp.pad(got, ((0, 0), (0, 0), (0, groups - sent_groups), (0, 0)))
    direct = jnp.stack([jnp.roll(padded[g], g, axis=1) for g in range(groups)])
    direct = direct.reshape(det_total, det_total)
    group_of = jnp.arange(det_total, dtype=jnp.int32) // lanes
    use_direct = (group_of[None, :] - group_of[:, None]) % groups < sent_groups
    return jnp.where(use_direct, direct, direct.T)


def wafer_sum(x):
    size = lax.axis_size("wafer")
    bit = 1
    while bit < size:
        x = x + lax.ppermute(x, "wafer", [(i, i ^ bit) for i in range(size)])
        bit *= 2
    return x


def shards(
    timestream,
    sample_weight,
    response,
    band_filter,
    whiten,
    group_wafer,
    pointing,
    tile_list,
    tile_home,
    solution,
    direction,
    cg_scalars,
):
    precise_mode = lax.Precision.HIGHEST
    tm_count = lax.axis_size("tm")
    tm_index = lax.axis_index("tm")
    step_size = cg_scalars[0]
    blend_weight = cg_scalars[1]
    updated = solution + step_size * direction
    short_map = updated.astype(jnp.bfloat16)
    tiles_own, comp_count, pixel_count = solution.shape
    spans_here, per_span = tile_list.shape
    samples = band_filter.shape[0]
    det_total = whiten.shape[2]
    row_count = spans_here * per_span
    capacity = max(2, (row_count + tm_count - 1) // tm_count)
    tile_ids = tile_list.reshape(row_count)
    home_rows = jnp.take(tile_home, tile_ids, axis=0)
    owners = home_rows // tiles_own
    local_slot = home_rows % tiles_own
    positions = jnp.arange(row_count, dtype=jnp.int32)
    earlier = (owners[:, None] == owners[None, :]) & (positions[None, :] < positions[:, None])
    before_count = jnp.sum(earlier.astype(jnp.int32), axis=1)
    targets = owners * capacity + before_count
    placing = targets[:, None] == jnp.arange(tm_count * capacity, dtype=jnp.int32)[None, :]
    requests = jnp.sum(jnp.where(placing, local_slot[:, None], 0), axis=0)
    requests = requests.reshape(tm_count, capacity)
    asked_slots = lax.all_to_all(requests, "tm", split_axis=0, concat_axis=0, tiled=True)
    served = jnp.take(short_map, asked_slots, axis=0)
    replies = lax.all_to_all(served, "tm", split_axis=0, concat_axis=0, tiled=True)
    fetched = jnp.take(
        replies.reshape(tm_count * capacity, comp_count, pixel_count), targets, axis=0
    )
    fetched = fetched.reshape(spans_here, per_span, comp_count, pixel_count)
    signal_parts = jnp.einsum(
        "cktp,ckjp->cjt", pointing, fetched, preferred_element_type=jnp.float32
    )
    block_rows = wafer_gather(whiten, 1)
    matrix = symmetric_gather(block_rows, group_wafer, tm_index, tm_count)
    columns = wafer_columns(timestream)
    column_weights = wafer_columns(sample_weight).astype(jnp.float32)
    width = spans_here * samples
    parts_flat = jnp.transpose(signal_parts, (1, 0, 2)).reshape(comp_count, width)
    signal = sum(response[j][:, None] * parts_flat[j][None, :] for j in range(comp_count))
    errors = ((columns.astype(jnp.float32) - signal) * column_weights).astype(jnp.bfloat16)
    block_id = jnp.arange(width, dtype=jnp.int32) // samples
    same_span = block_id[:, None] == block_id[None, :]
    filter_blocks = jnp.where(same_span, jnp.tile(band_filter, (spans_here, spans_here)), jnp.zeros((), band_filter.dtype))
    filtered = jnp.dot(errors, filter_blocks, preferred_element_type=jnp.float32).astype(jnp.bfloat16)
    whitened = jnp.dot(matrix, filtered, preferred_element_type=jnp.float32).astype(jnp.bfloat16)
    smoothed = lax.dot_general(
        whitened, filter_blocks, (((1,), (1,)), ((), ())), preferred_element_type=jnp.float32
    ).astype(jnp.bfloat16)
    weighted = smoothed.astype(jnp.float32) * column_weights
    stokes = jnp.stack([jnp.sum(response[j][:, None] * weighted, axis=0) for j in range(comp_count)])
    stokes_short = jnp.transpose(stokes.reshape(comp_count, spans_here, samples), (1, 0, 2)).astype(jnp.bfloat16)
    partial_value = jnp.einsum(
        "cjt,cktp->ckjp", stokes_short, pointing, preferred_element_type=jnp.float32
    )
    partial_value = partial_value.reshape(row_count, comp_count * pixel_count)
    outgoing = jnp.dot(placing.astype(jnp.float32).T, partial_value, precision=precise_mode)
    outgoing = outgoing.reshape(tm_count, capacity, comp_count, pixel_count)
    arrived = lax.all_to_all(outgoing, "tm", split_axis=0, concat_axis=0, tiled=True)
    slot_hits = (
        asked_slots.reshape(-1)[None, :] == jnp.arange(tiles_own, dtype=jnp.int32)[:, None]
    ).astype(jnp.float32)
    owned_sum = jnp.dot(
        slot_hits,
        arrived.reshape(tm_count * capacity, comp_count * pixel_count),
        precision=precise_mode,
    )
    owned_sum = owned_sum.reshape(tiles_own, comp_count, pixel_count)
    summed = wafer_sum(owned_sum)
    residual_next = summed * float(det_total) ** (-0.5)
    direction_next = residual_next + blend_weight * direction
    return (updated, residual_next, direction_next)


def solution(mesh):
    in_specs = (
        P("wafer", "tm"),
        P("wafer", "tm"),
        P(),
        P(),
        P(None, ("tm", "wafer"), None),
        P(),
        P(("tm", "wafer"), None, None, None),
        P(("tm", "wafer"), None),
        P(),
        P("tm", None, None),
        P("tm", None, None),
        P(),
    )
    out_specs = (P("tm", None, None), P("tm", None, None), P("tm", None, None))

    return jax.shard_map(shards, mesh=mesh, in_specs=in_specs, out_specs=out_specs, check_vma=False)
```

```python
import jax
import jax.numpy as jnp
from jax import lax
from jax.sharding import PartitionSpec as P


def wafer_gather(x, axis):
    spot = lax.axis_index("wafer")
    size = lax.axis_size("wafer")
    bit = 1
    while bit < size:
        other = lax.ppermute(x, "wafer", [(i, i ^ bit) for i in range(size)])
        low = (spot & bit) == 0
        x = jnp.where(low, jnp.concatenate([x, other], axis), jnp.concatenate([other, x], axis))
        bit *= 2
    return x


def wafer_columns(x):
    spot = lax.axis_index("wafer")
    size = lax.axis_size("wafer")
    width = x.shape[1] // size
    pieces = [lax.dynamic_slice_in_dim(x, spot * width, width, 1)]
    for shift in range(1, size):
        target = (spot + shift) % size
        piece = lax.dynamic_slice_in_dim(x, target * width, width, 1)
        pieces.append(lax.ppermute(piece, "wafer", [(i, (i + shift) % size) for i in range(size)]))
    rows = x.shape[0]
    placed = jnp.zeros((size, rows, width), x.dtype)
    for shift, piece in enumerate(pieces):
        source = (spot - shift) % size
        placed = lax.dynamic_update_slice_in_dim(placed, piece[None], source, 0)
    return placed.reshape(size * rows, width)


def wafer_sum(x):
    spot = lax.axis_index("wafer")
    size = lax.axis_size("wafer")
    terms = [x]
    for shift in range(1, size):
        terms.append(lax.ppermute(x, "wafer", [(i, (i + shift) % size) for i in range(size)]))
    total = None
    for source in range(size):
        term = terms[0]
        for shift in range(1, size):
            term = jnp.where((spot - source) % size == shift, terms[shift], term)
        total = term if total is None else total + term
    return total


def shards(
    timestream,
    sample_weight,
    response,
    band_filter,
    whiten,
    group_wafer,
    pointing,
    tile_list,
    tile_home,
    solution,
    direction,
    cg_scalars,
):
    precise_mode = lax.Precision.HIGHEST
    tm_count = lax.axis_size("tm")
    tm_index = lax.axis_index("tm")
    step_size = cg_scalars[0]
    blend_weight = cg_scalars[1]
    updated = solution + step_size * direction
    short_map = updated.astype(jnp.bfloat16)
    tiles_own, comp_count, pixel_count = solution.shape
    spans_here, per_span = tile_list.shape
    samples = band_filter.shape[0]
    det_total = whiten.shape[2]
    row_count = spans_here * per_span
    capacity = max(2, (row_count + tm_count - 1) // tm_count)
    tile_ids = tile_list.reshape(row_count)
    home_rows = jnp.take(tile_home, tile_ids, axis=0)
    owners = home_rows // tiles_own
    local_slot = home_rows % tiles_own
    positions = jnp.arange(row_count, dtype=jnp.int32)
    earlier = (owners[:, None] == owners[None, :]) & (positions[None, :] < positions[:, None])
    before_count = jnp.sum(earlier.astype(jnp.int32), axis=1)
    targets = owners * capacity + before_count
    placing = targets[:, None] == jnp.arange(tm_count * capacity, dtype=jnp.int32)[None, :]
    requests = jnp.sum(jnp.where(placing, local_slot[:, None], 0), axis=0)
    requests = requests.reshape(tm_count, capacity)
    asked_slots = lax.all_to_all(requests, "tm", split_axis=0, concat_axis=0, tiled=True)
    served = jnp.take(short_map, asked_slots, axis=0)
    replies, asked_slots = (
        lax.all_to_all(served, "tm", split_axis=0, concat_axis=0, tiled=True),
        asked_slots,
    )
    fetched = jnp.take(
        replies.reshape(tm_count * capacity, comp_count, pixel_count), targets, axis=0
    )
    fetched = fetched.reshape(spans_here, per_span, comp_count, pixel_count)
    signal_parts = jnp.einsum(
        "cktp,ckjp->cjt", pointing, fetched, preferred_element_type=jnp.float32
    )
    block_rows = wafer_gather(whiten, 1)
    sent_blocks = jnp.take(block_rows, group_wafer, axis=0)
    matrix = lax.all_to_all(sent_blocks, "tm", split_axis=0, concat_axis=0, tiled=True)
    matrix = matrix.reshape(det_total, det_total)
    columns = wafer_columns(timestream)
    column_weights = wafer_columns(sample_weight).astype(jnp.float32)
    width = spans_here * samples
    parts_flat = jnp.transpose(signal_parts, (1, 0, 2)).reshape(comp_count, width)
    signal = sum(response[j][:, None] * parts_flat[j][None, :] for j in range(comp_count))
    errors = ((columns.astype(jnp.float32) - signal) * column_weights).astype(jnp.bfloat16)
    block_id = jnp.arange(width, dtype=jnp.int32) // samples
    same_span = block_id[:, None] == block_id[None, :]
    filter_blocks = jnp.where(same_span, jnp.tile(band_filter, (spans_here, spans_here)), jnp.zeros((), band_filter.dtype))
    filtered = jnp.dot(errors, filter_blocks, preferred_element_type=jnp.float32).astype(jnp.bfloat16)
    whitened = jnp.dot(matrix, filtered, preferred_element_type=jnp.float32).astype(jnp.bfloat16)
    smoothed = lax.dot_general(
        whitened, filter_blocks, (((1,), (1,)), ((), ())), preferred_element_type=jnp.float32
    ).astype(jnp.bfloat16)
    weighted = smoothed.astype(jnp.float32) * column_weights
    stokes = jnp.stack([jnp.sum(response[j][:, None] * weighted, axis=0) for j in range(comp_count)])
    stokes_short = jnp.transpose(stokes.reshape(comp_count, spans_here, samples), (1, 0, 2)).astype(jnp.bfloat16)
    partial_value = jnp.einsum(
        "cjt,cktp->ckjp", stokes_short, pointing, preferred_element_type=jnp.float32
    )
    partial_value = partial_value.reshape(row_count, comp_count * pixel_count)
    outgoing = jnp.dot(placing.astype(jnp.float32).T, partial_value, precision=precise_mode)
    outgoing = outgoing.reshape(tm_count, capacity, comp_count, pixel_count)
    arrived = lax.all_to_all(outgoing, "tm", split_axis=0, concat_axis=0, tiled=True)
    slot_hits = (
        asked_slots.reshape(-1)[None, :] == jnp.arange(tiles_own, dtype=jnp.int32)[:, None]
    ).astype(jnp.float32)
    owned_sum = jnp.dot(
        slot_hits,
        arrived.reshape(tm_count * capacity, comp_count * pixel_count),
        precision=precise_mode,
    )
    owned_sum = owned_sum.reshape(tiles_own, comp_count, pixel_count)
    summed = wafer_sum(owned_sum)
    residual_next = summed * float(det_total) ** (-0.5)
    direction_next = residual_next + blend_weight * direction
    return (updated, residual_next, direction_next)


def solution(mesh):
    in_specs = (
        P("wafer", "tm"),
        P("wafer", "tm"),
        P(),
        P(),
        P(None, ("tm", "wafer"), None),
        P(),
        P(("tm", "wafer"), None, None, None),
        P(("tm", "wafer"), None),
        P(),
        P("tm", None, None),
        P("tm", None, None),
        P(),
    )
    out_specs = (P("tm", None, None), P("tm", None, None), P("tm", None, None))
    return jax.shard_map(shards, mesh=mesh, in_specs=in_specs, out_specs=out_specs, check_vma=False)
```

```python
import jax
import jax.numpy as jnp
from jax import lax
from jax.sharding import PartitionSpec as P


def wafer_gather(x, axis):
    spot = lax.axis_index("wafer")
    size = lax.axis_size("wafer")
    bit = 1
    while bit < size:
        other = lax.ppermute(x, "wafer", [(i, i ^ bit) for i in range(size)])
        low = (spot & bit) == 0
        x = jnp.where(low, jnp.concatenate([x, other], axis), jnp.concatenate([other, x], axis))
        bit *= 2
    return x


def wafer_columns(x):
    spot = lax.axis_index("wafer")
    size = lax.axis_size("wafer")
    width = x.shape[1] // size
    pieces = [lax.dynamic_slice_in_dim(x, spot * width, width, 1)]
    for shift in range(1, size):
        target = (spot + shift) % size
        piece = lax.dynamic_slice_in_dim(x, target * width, width, 1)
        pieces.append(lax.ppermute(piece, "wafer", [(i, (i + shift) % size) for i in range(size)]))
    rows = x.shape[0]
    placed = jnp.zeros((size, rows, width), x.dtype)
    for shift, piece in enumerate(pieces):
        source = (spot - shift) % size
        placed = lax.dynamic_update_slice_in_dim(placed, piece[None], source, 0)
    return placed.reshape(size * rows, width)


def wafer_sum(x):
    spot = lax.axis_index("wafer")
    size = lax.axis_size("wafer")
    terms = [x]
    for shift in range(1, size):
        terms.append(lax.ppermute(x, "wafer", [(i, (i + shift) % size) for i in range(size)]))
    total = None
    for source in range(size):
        term = terms[0]
        for shift in range(1, size):
            term = jnp.where((spot - source) % size == shift, terms[shift], term)
        total = term if total is None else total + term
    return total


def shards(
    timestream,
    sample_weight,
    response,
    band_filter,
    whiten,
    group_wafer,
    pointing,
    tile_list,
    tile_home,
    solution,
    direction,
    cg_scalars,
):
    precise_mode = lax.Precision.HIGHEST
    tm_count = lax.axis_size("tm")
    tm_index = lax.axis_index("tm")
    step_size = cg_scalars[0]
    blend_weight = cg_scalars[1]
    updated = solution + step_size * direction
    short_map = updated.astype(jnp.bfloat16)
    tiles_own, comp_count, pixel_count = solution.shape
    spans_here, per_span = tile_list.shape
    samples = band_filter.shape[0]
    det_total = whiten.shape[2]
    row_count = spans_here * per_span
    capacity = max(2, (row_count + tm_count - 1) // tm_count)
    tile_ids = tile_list.reshape(row_count)
    home_rows = jnp.take(tile_home, tile_ids, axis=0)
    owners = home_rows // tiles_own
    local_slot = home_rows % tiles_own
    positions = jnp.arange(row_count, dtype=jnp.int32)
    earlier = (owners[:, None] == owners[None, :]) & (positions[None, :] < positions[:, None])
    before_count = jnp.sum(earlier.astype(jnp.int32), axis=1)
    targets = owners * capacity + before_count
    placing = targets[:, None] == jnp.arange(tm_count * capacity, dtype=jnp.int32)[None, :]
    requests = jnp.sum(jnp.where(placing, local_slot[:, None], 0), axis=0)
    requests = requests.reshape(tm_count, capacity)
    asked_slots = lax.all_to_all(requests, "tm", split_axis=0, concat_axis=0, tiled=True)
    served = jnp.take(short_map, asked_slots, axis=0)
    replies, asked_slots = (
        lax.all_to_all(served, "tm", split_axis=0, concat_axis=0, tiled=True),
        asked_slots,
    )
    fetched = jnp.take(
        replies.reshape(tm_count * capacity, comp_count, pixel_count), targets, axis=0
    )
    fetched = fetched.reshape(spans_here, per_span, comp_count, pixel_count)
    signal_parts = jnp.einsum(
        "cktp,ckjp->cjt", pointing, fetched, preferred_element_type=jnp.float32
    )
    block_rows = wafer_gather(whiten, 1)
    sent_blocks = jnp.take(block_rows, group_wafer, axis=0)
    matrix = lax.all_to_all(sent_blocks, "tm", split_axis=0, concat_axis=0, tiled=True)
    matrix = matrix.reshape(det_total, det_total)
    columns = wafer_columns(timestream)
    column_weights = wafer_columns(sample_weight).astype(jnp.float32)
    width = spans_here * samples
    parts_flat = jnp.transpose(signal_parts, (1, 0, 2)).reshape(comp_count, width)
    signal = sum(response[j][:, None] * parts_flat[j][None, :] for j in range(comp_count))
    errors = ((columns.astype(jnp.float32) - signal) * column_weights).astype(jnp.bfloat16)
    block_id = jnp.arange(width, dtype=jnp.int32) // samples
    same_span = block_id[:, None] == block_id[None, :]
    filter_blocks = jnp.where(same_span, jnp.tile(band_filter, (spans_here, spans_here)), jnp.zeros((), band_filter.dtype))
    filtered = jnp.dot(errors, filter_blocks, preferred_element_type=jnp.float32).astype(jnp.bfloat16)
    whitened = jnp.dot(matrix, filtered, preferred_element_type=jnp.float32).astype(jnp.bfloat16)
    smoothed = lax.dot_general(
        whitened, filter_blocks, (((1,), (1,)), ((), ())), preferred_element_type=jnp.float32
    ).astype(jnp.bfloat16)
    weighted = smoothed.astype(jnp.float32) * column_weights
    tile_rows = 8
    blocks = [
        jnp.sum((response[j][:, None] * weighted).reshape(det_total // tile_rows, tile_rows, width), axis=0)
        for j in range(comp_count)
    ]
    stokes = jnp.sum(lax.optimization_barrier(jnp.stack(blocks)), axis=1)
    stokes_short = jnp.transpose(stokes.reshape(comp_count, spans_here, samples), (1, 0, 2)).astype(jnp.bfloat16)
    partial_value = jnp.einsum(
        "cjt,cktp->ckjp", stokes_short, pointing, preferred_element_type=jnp.float32
    )
    partial_value = partial_value.reshape(row_count, comp_count * pixel_count)
    outgoing = jnp.dot(placing.astype(jnp.float32).T, partial_value, precision=precise_mode)
    outgoing = outgoing.reshape(tm_count, capacity, comp_count, pixel_count)
    arrived = lax.all_to_all(outgoing, "tm", split_axis=0, concat_axis=0, tiled=True)
    slot_hits = (
        asked_slots.reshape(-1)[None, :] == jnp.arange(tiles_own, dtype=jnp.int32)[:, None]
    ).astype(jnp.float32)
    owned_sum = jnp.dot(
        slot_hits,
        arrived.reshape(tm_count * capacity, comp_count * pixel_count),
        precision=precise_mode,
    )
    owned_sum = owned_sum.reshape(tiles_own, comp_count, pixel_count)
    summed = wafer_sum(owned_sum)
    residual_next = summed * float(det_total) ** (-0.5)
    direction_next = residual_next + blend_weight * direction
    return (updated, residual_next, direction_next)


def solution(mesh):
    in_specs = (
        P("wafer", "tm"),
        P("wafer", "tm"),
        P(),
        P(),
        P(None, ("tm", "wafer"), None),
        P(),
        P(("tm", "wafer"), None, None, None),
        P(("tm", "wafer"), None),
        P(),
        P("tm", None, None),
        P("tm", None, None),
        P(),
    )
    out_specs = (P("tm", None, None), P("tm", None, None), P("tm", None, None))
    return jax.shard_map(shards, mesh=mesh, in_specs=in_specs, out_specs=out_specs, check_vma=False)
```

```python
import jax
import jax.numpy as jnp
from jax import lax
from jax.sharding import PartitionSpec as P


def wafer_gather(x, axis):
    spot = lax.axis_index("wafer")
    size = lax.axis_size("wafer")
    bit = 1
    while bit < size:
        other = lax.ppermute(x, "wafer", [(i, i ^ bit) for i in range(size)])
        low = (spot & bit) == 0
        x = jnp.where(low, jnp.concatenate([x, other], axis), jnp.concatenate([other, x], axis))
        bit *= 2
    return x


def wafer_columns(x):
    spot = lax.axis_index("wafer")
    size = lax.axis_size("wafer")
    width = x.shape[1] // size
    pieces = [lax.dynamic_slice_in_dim(x, spot * width, width, 1)]
    for shift in range(1, size):
        target = (spot + shift) % size
        piece = lax.dynamic_slice_in_dim(x, target * width, width, 1)
        pieces.append(lax.ppermute(piece, "wafer", [(i, (i + shift) % size) for i in range(size)]))
    rows = x.shape[0]
    placed = jnp.zeros((size, rows, width), x.dtype)
    for shift, piece in enumerate(pieces):
        source = (spot - shift) % size
        placed = lax.dynamic_update_slice_in_dim(placed, piece[None], source, 0)
    return placed.reshape(size * rows, width)


def wafer_sum(x):
    spot = lax.axis_index("wafer")
    size = lax.axis_size("wafer")
    terms = [x]
    for shift in range(1, size):
        terms.append(lax.ppermute(x, "wafer", [(i, (i + shift) % size) for i in range(size)]))
    total = None
    for source in range(size):
        term = terms[0]
        for shift in range(1, size):
            term = jnp.where((spot - source) % size == shift, terms[shift], term)
        total = term if total is None else total + term
    return total


def shards(
    timestream,
    sample_weight,
    response,
    band_filter,
    whiten,
    group_wafer,
    pointing,
    tile_list,
    tile_home,
    solution,
    direction,
    cg_scalars,
):
    precise_mode = lax.Precision.HIGHEST
    tm_count = lax.axis_size("tm")
    tm_index = lax.axis_index("tm")
    step_size = cg_scalars[0]
    blend_weight = cg_scalars[1]
    updated = solution + step_size * direction
    short_map = updated.astype(jnp.bfloat16)
    tiles_own, comp_count, pixel_count = solution.shape
    spans_here, per_span = tile_list.shape
    samples = band_filter.shape[0]
    det_total = whiten.shape[2]
    row_count = spans_here * per_span
    capacity = max(2, (row_count + tm_count - 1) // tm_count)
    tile_ids = tile_list.reshape(row_count)
    home_rows = jnp.take(tile_home, tile_ids, axis=0)
    owners = home_rows // tiles_own
    local_slot = home_rows % tiles_own
    positions = jnp.arange(row_count, dtype=jnp.int32)
    earlier = (owners[:, None] == owners[None, :]) & (positions[None, :] < positions[:, None])
    before_count = jnp.sum(earlier.astype(jnp.int32), axis=1)
    targets = owners * capacity + before_count
    placing = targets[:, None] == jnp.arange(tm_count * capacity, dtype=jnp.int32)[None, :]
    requests = jnp.sum(jnp.where(placing, local_slot[:, None], 0), axis=0)
    requests = requests.reshape(tm_count, capacity)
    asked_slots = lax.all_to_all(requests, "tm", split_axis=0, concat_axis=0, tiled=True)
    served = jnp.take(short_map, asked_slots, axis=0)
    replies, asked_slots = (
        lax.all_to_all(served, "tm", split_axis=0, concat_axis=0, tiled=True),
        asked_slots,
    )
    fetched = jnp.take(
        replies.reshape(tm_count * capacity, comp_count, pixel_count), targets, axis=0
    )
    fetched = fetched.reshape(spans_here, per_span, comp_count, pixel_count)
    signal_parts = jnp.einsum(
        "cktp,ckjp->cjt", pointing, fetched, preferred_element_type=jnp.float32
    )
    block_rows = wafer_gather(whiten, 1)
    sent_blocks = jnp.take(block_rows, group_wafer, axis=0)
    matrix = lax.all_to_all(sent_blocks, "tm", split_axis=0, concat_axis=0, tiled=True)
    matrix = matrix.reshape(det_total, det_total)
    columns = wafer_columns(timestream)
    column_weights = wafer_columns(sample_weight).astype(jnp.float32)
    width = spans_here * samples
    parts_flat = jnp.transpose(signal_parts, (1, 0, 2)).reshape(comp_count, width)
    signal = sum(response[j][:, None] * parts_flat[j][None, :] for j in range(comp_count))
    errors = ((columns.astype(jnp.float32) - signal) * column_weights).astype(jnp.bfloat16)
    stokes_spans = []
    for c in range(spans_here):
        span = slice(c * samples, (c + 1) * samples)
        filtered = jnp.dot(errors[:, span], band_filter, preferred_element_type=jnp.float32).astype(jnp.bfloat16)
        whitened = jnp.dot(matrix, filtered, preferred_element_type=jnp.float32).astype(jnp.bfloat16)
        smoothed = lax.dot_general(
            whitened, band_filter, (((1,), (1,)), ((), ())), preferred_element_type=jnp.float32
        ).astype(jnp.bfloat16)
        weighted = smoothed.astype(jnp.float32) * column_weights[:, span]
        stokes_spans.append(jnp.stack([jnp.sum(response[j][:, None] * weighted, axis=0) for j in range(comp_count)]))
    stokes_short = jnp.stack(stokes_spans).astype(jnp.bfloat16)
    partial_value = jnp.einsum(
        "cjt,cktp->ckjp", stokes_short, pointing, preferred_element_type=jnp.float32
    )
    partial_value = partial_value.reshape(row_count, comp_count * pixel_count)
    outgoing = jnp.dot(placing.astype(jnp.float32).T, partial_value, precision=precise_mode)
    outgoing = outgoing.reshape(tm_count, capacity, comp_count, pixel_count)
    arrived = lax.all_to_all(outgoing, "tm", split_axis=0, concat_axis=0, tiled=True)
    slot_hits = (
        asked_slots.reshape(-1)[None, :] == jnp.arange(tiles_own, dtype=jnp.int32)[:, None]
    ).astype(jnp.float32)
    owned_sum = jnp.dot(
        slot_hits,
        arrived.reshape(tm_count * capacity, comp_count * pixel_count),
        precision=precise_mode,
    )
    owned_sum = owned_sum.reshape(tiles_own, comp_count, pixel_count)
    summed = wafer_sum(owned_sum)
    residual_next = summed * float(det_total) ** (-0.5)
    direction_next = residual_next + blend_weight * direction
    return (updated, residual_next, direction_next)


def solution(mesh):
    in_specs = (
        P("wafer", "tm"),
        P("wafer", "tm"),
        P(),
        P(),
        P(None, ("tm", "wafer"), None),
        P(),
        P(("tm", "wafer"), None, None, None),
        P(("tm", "wafer"), None),
        P(),
        P("tm", None, None),
        P("tm", None, None),
        P(),
    )
    out_specs = (P("tm", None, None), P("tm", None, None), P("tm", None, None))
    return jax.shard_map(shards, mesh=mesh, in_specs=in_specs, out_specs=out_specs, check_vma=False)
```

```python
import jax
import jax.numpy as jnp
from jax import lax
from jax.sharding import PartitionSpec as P


def wafer_gather(x, axis):
    spot = lax.axis_index("wafer")
    size = lax.axis_size("wafer")
    bit = 1
    while bit < size:
        other = lax.ppermute(x, "wafer", [(i, i ^ bit) for i in range(size)])
        low = (spot & bit) == 0
        x = jnp.where(low, jnp.concatenate([x, other], axis), jnp.concatenate([other, x], axis))
        bit *= 2
    return x


def wafer_columns(x):
    spot = lax.axis_index("wafer")
    size = lax.axis_size("wafer")
    width = x.shape[1] // size
    pieces = [lax.dynamic_slice_in_dim(x, spot * width, width, 1)]
    for shift in range(1, size):
        target = (spot + shift) % size
        piece = lax.dynamic_slice_in_dim(x, target * width, width, 1)
        pieces.append(lax.ppermute(piece, "wafer", [(i, (i + shift) % size) for i in range(size)]))
    rows = x.shape[0]
    placed = jnp.zeros((size, rows, width), x.dtype)
    for shift, piece in enumerate(pieces):
        source = (spot - shift) % size
        placed = lax.dynamic_update_slice_in_dim(placed, piece[None], source, 0)
    return placed.reshape(size * rows, width)


def wafer_sum(x):
    spot = lax.axis_index("wafer")
    size = lax.axis_size("wafer")
    terms = [x]
    for shift in range(1, size):
        terms.append(lax.ppermute(x, "wafer", [(i, (i + shift) % size) for i in range(size)]))
    total = None
    for source in range(size):
        term = terms[0]
        for shift in range(1, size):
            term = jnp.where((spot - source) % size == shift, terms[shift], term)
        total = term if total is None else total + term
    return total


def shards(
    timestream,
    sample_weight,
    response,
    band_filter,
    whiten,
    group_wafer,
    pointing,
    tile_list,
    tile_home,
    solution,
    direction,
    cg_scalars,
):
    precise_mode = lax.Precision.HIGHEST
    tm_count = lax.axis_size("tm")
    tm_index = lax.axis_index("tm")
    step_size = cg_scalars[0]
    blend_weight = cg_scalars[1]
    updated = solution + step_size * direction
    short_map = updated.astype(jnp.bfloat16)
    tiles_own, comp_count, pixel_count = solution.shape
    spans_here, per_span = tile_list.shape
    samples = band_filter.shape[0]
    det_total = whiten.shape[2]
    row_count = spans_here * per_span
    capacity = max(2, (row_count + tm_count - 1) // tm_count)
    tile_ids = tile_list.reshape(row_count)
    home_rows = jnp.take(tile_home, tile_ids, axis=0)
    owners = home_rows // tiles_own
    local_slot = home_rows % tiles_own
    positions = jnp.arange(row_count, dtype=jnp.int32)
    earlier = (owners[:, None] == owners[None, :]) & (positions[None, :] < positions[:, None])
    before_count = jnp.sum(earlier.astype(jnp.int32), axis=1)
    targets = owners * capacity + before_count
    placing = targets[:, None] == jnp.arange(tm_count * capacity, dtype=jnp.int32)[None, :]
    requests = jnp.sum(jnp.where(placing, local_slot[:, None], 0), axis=0)
    requests = requests.reshape(tm_count, capacity)
    asked_slots = lax.all_to_all(requests, "tm", split_axis=0, concat_axis=0, tiled=True)
    served = jnp.take(short_map, asked_slots, axis=0)
    block_rows = wafer_gather(whiten, 1)
    sent_blocks = jnp.take(block_rows, group_wafer, axis=0).reshape(tm_count, -1)
    block_size = sent_blocks.shape[1]
    packed = jnp.concatenate([sent_blocks, served.reshape(tm_count, -1)], axis=1)
    unpacked = lax.all_to_all(packed, "tm", split_axis=0, concat_axis=0, tiled=True)
    matrix = unpacked[:, :block_size].reshape(det_total, det_total)
    replies = unpacked[:, block_size:].reshape(tm_count, capacity, comp_count, pixel_count)
    fetched = jnp.take(
        replies.reshape(tm_count * capacity, comp_count, pixel_count), targets, axis=0
    )
    fetched = fetched.reshape(spans_here, per_span, comp_count, pixel_count)
    signal_parts = jnp.einsum(
        "cktp,ckjp->cjt", pointing, fetched, preferred_element_type=jnp.float32
    )
    columns = wafer_columns(timestream)
    column_weights = wafer_columns(sample_weight).astype(jnp.float32)
    width = spans_here * samples
    parts_flat = jnp.transpose(signal_parts, (1, 0, 2)).reshape(comp_count, width)
    signal = sum(response[j][:, None] * parts_flat[j][None, :] for j in range(comp_count))
    errors = ((columns.astype(jnp.float32) - signal) * column_weights).astype(jnp.bfloat16)
    block_id = jnp.arange(width, dtype=jnp.int32) // samples
    same_span = block_id[:, None] == block_id[None, :]
    filter_blocks = jnp.where(same_span, jnp.tile(band_filter, (spans_here, spans_here)), jnp.zeros((), band_filter.dtype))
    filtered = jnp.dot(errors, filter_blocks, preferred_element_type=jnp.float32).astype(jnp.bfloat16)
    whitened = jnp.dot(matrix, filtered, preferred_element_type=jnp.float32).astype(jnp.bfloat16)
    smoothed = lax.dot_general(
        whitened, filter_blocks, (((1,), (1,)), ((), ())), preferred_element_type=jnp.float32
    ).astype(jnp.bfloat16)
    weighted = smoothed.astype(jnp.float32) * column_weights
    stokes = jnp.stack([jnp.sum(response[j][:, None] * weighted, axis=0) for j in range(comp_count)])
    stokes_short = jnp.transpose(stokes.reshape(comp_count, spans_here, samples), (1, 0, 2)).astype(jnp.bfloat16)
    partial_value = jnp.einsum(
        "cjt,cktp->ckjp", stokes_short, pointing, preferred_element_type=jnp.float32
    )
    partial_value = partial_value.reshape(row_count, comp_count * pixel_count)
    outgoing = jnp.dot(placing.astype(jnp.float32).T, partial_value, precision=precise_mode)
    outgoing = outgoing.reshape(tm_count, capacity, comp_count, pixel_count)
    arrived = lax.all_to_all(outgoing, "tm", split_axis=0, concat_axis=0, tiled=True)
    slot_hits = (
        asked_slots.reshape(-1)[None, :] == jnp.arange(tiles_own, dtype=jnp.int32)[:, None]
    ).astype(jnp.float32)
    owned_sum = jnp.dot(
        slot_hits,
        arrived.reshape(tm_count * capacity, comp_count * pixel_count),
        precision=precise_mode,
    )
    owned_sum = owned_sum.reshape(tiles_own, comp_count, pixel_count)
    summed = wafer_sum(owned_sum)
    residual_next = summed * float(det_total) ** (-0.5)
    direction_next = residual_next + blend_weight * direction
    return (updated, residual_next, direction_next)


def solution(mesh):
    in_specs = (
        P("wafer", "tm"),
        P("wafer", "tm"),
        P(),
        P(),
        P(None, ("tm", "wafer"), None),
        P(),
        P(("tm", "wafer"), None, None, None),
        P(("tm", "wafer"), None),
        P(),
        P("tm", None, None),
        P("tm", None, None),
        P(),
    )
    out_specs = (P("tm", None, None), P("tm", None, None), P("tm", None, None))
    return jax.shard_map(shards, mesh=mesh, in_specs=in_specs, out_specs=out_specs, check_vma=False)
```

```python
import jax
import jax.numpy as jnp
from jax import lax
from jax.sharding import PartitionSpec as P


def wafer_gather(x, axis):
    spot = lax.axis_index("wafer")
    size = lax.axis_size("wafer")
    bit = 1
    while bit < size:
        other = lax.ppermute(x, "wafer", [(i, i ^ bit) for i in range(size)])
        low = (spot & bit) == 0
        x = jnp.where(low, jnp.concatenate([x, other], axis), jnp.concatenate([other, x], axis))
        bit *= 2
    return x


def wafer_columns(x):
    spot = lax.axis_index("wafer")
    size = lax.axis_size("wafer")
    width = x.shape[1] // size
    pieces = [lax.dynamic_slice_in_dim(x, spot * width, width, 1)]
    for shift in range(1, size):
        target = (spot + shift) % size
        piece = lax.dynamic_slice_in_dim(x, target * width, width, 1)
        pieces.append(lax.ppermute(piece, "wafer", [(i, (i + shift) % size) for i in range(size)]))
    rows = x.shape[0]
    placed = jnp.zeros((size, rows, width), x.dtype)
    for shift, piece in enumerate(pieces):
        source = (spot - shift) % size
        placed = lax.dynamic_update_slice_in_dim(placed, piece[None], source, 0)
    return placed.reshape(size * rows, width)


def symmetric_gather(block_rows, group_wafer, tm_index, tm_count):
    _, rows, det_total = block_rows.shape
    groups = 8
    lanes = det_total // groups
    sent_groups = groups // 2 + 1
    home_group = tm_index // (tm_count // groups)
    rolled = jnp.roll(block_rows, -home_group * lanes, axis=2)[:, :, : sent_groups * lanes]
    sent = jnp.take(rolled, group_wafer, axis=0)
    got = lax.all_to_all(sent, "tm", split_axis=0, concat_axis=0, tiled=True)
    got = got.reshape(groups, det_total // groups, sent_groups, lanes)
    padded = jnp.pad(got, ((0, 0), (0, 0), (0, groups - sent_groups), (0, 0)))
    direct = jnp.stack([jnp.roll(padded[g], g, axis=1) for g in range(groups)])
    direct = direct.reshape(det_total, det_total)
    group_of = jnp.arange(det_total, dtype=jnp.int32) // lanes
    use_direct = (group_of[None, :] - group_of[:, None]) % groups < sent_groups
    return lax.optimization_barrier(jnp.where(use_direct, direct, direct.T))


def wafer_sum(x):
    spot = lax.axis_index("wafer")
    size = lax.axis_size("wafer")
    terms = [x]
    for shift in range(1, size):
        terms.append(lax.ppermute(x, "wafer", [(i, (i + shift) % size) for i in range(size)]))
    total = None
    for source in range(size):
        term = terms[0]
        for shift in range(1, size):
            term = jnp.where((spot - source) % size == shift, terms[shift], term)
        total = term if total is None else total + term
    return total


def shards(
    timestream,
    sample_weight,
    response,
    band_filter,
    whiten,
    group_wafer,
    pointing,
    tile_list,
    tile_home,
    solution,
    direction,
    cg_scalars,
):
    precise_mode = lax.Precision.HIGHEST
    tm_count = lax.axis_size("tm")
    tm_index = lax.axis_index("tm")
    step_size = cg_scalars[0]
    blend_weight = cg_scalars[1]
    updated = solution + step_size * direction
    short_map = updated.astype(jnp.bfloat16)
    tiles_own, comp_count, pixel_count = solution.shape
    spans_here, per_span = tile_list.shape
    samples = band_filter.shape[0]
    det_total = whiten.shape[2]
    row_count = spans_here * per_span
    capacity = max(2, (row_count + tm_count - 1) // tm_count)
    tile_ids = tile_list.reshape(row_count)
    home_rows = jnp.take(tile_home, tile_ids, axis=0)
    owners = home_rows // tiles_own
    local_slot = home_rows % tiles_own
    positions = jnp.arange(row_count, dtype=jnp.int32)
    earlier = (owners[:, None] == owners[None, :]) & (positions[None, :] < positions[:, None])
    before_count = jnp.sum(earlier.astype(jnp.int32), axis=1)
    targets = owners * capacity + before_count
    placing = targets[:, None] == jnp.arange(tm_count * capacity, dtype=jnp.int32)[None, :]
    requests = jnp.sum(jnp.where(placing, local_slot[:, None], 0), axis=0)
    requests = requests.reshape(tm_count, capacity)
    asked_slots = lax.all_to_all(requests, "tm", split_axis=0, concat_axis=0, tiled=True)
    served = jnp.take(short_map, asked_slots, axis=0)
    replies, asked_slots = (
        lax.all_to_all(served, "tm", split_axis=0, concat_axis=0, tiled=True),
        asked_slots,
    )
    fetched = jnp.take(
        replies.reshape(tm_count * capacity, comp_count, pixel_count), targets, axis=0
    )
    fetched = fetched.reshape(spans_here, per_span, comp_count, pixel_count)
    signal_parts = jnp.einsum(
        "cktp,ckjp->cjt", pointing, fetched, preferred_element_type=jnp.float32
    )
    block_rows = wafer_gather(whiten, 1)
    matrix = symmetric_gather(block_rows, group_wafer, tm_index, tm_count)
    columns = wafer_columns(timestream)
    column_weights = wafer_columns(sample_weight).astype(jnp.float32)
    width = spans_here * samples
    parts_flat = jnp.transpose(signal_parts, (1, 0, 2)).reshape(comp_count, width)
    signal = sum(response[j][:, None] * parts_flat[j][None, :] for j in range(comp_count))
    errors = ((columns.astype(jnp.float32) - signal) * column_weights).astype(jnp.bfloat16)
    block_id = jnp.arange(width, dtype=jnp.int32) // samples
    same_span = block_id[:, None] == block_id[None, :]
    filter_blocks = jnp.where(same_span, jnp.tile(band_filter, (spans_here, spans_here)), jnp.zeros((), band_filter.dtype))
    filtered = jnp.dot(errors, filter_blocks, preferred_element_type=jnp.float32).astype(jnp.bfloat16)
    whitened = jnp.dot(matrix, filtered, preferred_element_type=jnp.float32).astype(jnp.bfloat16)
    smoothed = lax.dot_general(
        whitened, filter_blocks, (((1,), (1,)), ((), ())), preferred_element_type=jnp.float32
    ).astype(jnp.bfloat16)
    weighted = smoothed.astype(jnp.float32) * column_weights
    stokes = jnp.stack([jnp.sum(response[j][:, None] * weighted, axis=0) for j in range(comp_count)])
    stokes_short = jnp.transpose(stokes.reshape(comp_count, spans_here, samples), (1, 0, 2)).astype(jnp.bfloat16)
    partial_value = jnp.einsum(
        "cjt,cktp->ckjp", stokes_short, pointing, preferred_element_type=jnp.float32
    )
    partial_value = partial_value.reshape(row_count, comp_count * pixel_count)
    outgoing = jnp.dot(placing.astype(jnp.float32).T, partial_value, precision=precise_mode)
    outgoing = outgoing.reshape(tm_count, capacity, comp_count, pixel_count)
    arrived = lax.all_to_all(outgoing, "tm", split_axis=0, concat_axis=0, tiled=True)
    slot_hits = (
        asked_slots.reshape(-1)[None, :] == jnp.arange(tiles_own, dtype=jnp.int32)[:, None]
    ).astype(jnp.float32)
    owned_sum = jnp.dot(
        slot_hits,
        arrived.reshape(tm_count * capacity, comp_count * pixel_count),
        precision=precise_mode,
    )
    owned_sum = owned_sum.reshape(tiles_own, comp_count, pixel_count)
    summed = wafer_sum(owned_sum)
    residual_next = summed * float(det_total) ** (-0.5)
    direction_next = residual_next + blend_weight * direction
    return (updated, residual_next, direction_next)


def solution(mesh):
    in_specs = (
        P("wafer", "tm"),
        P("wafer", "tm"),
        P(),
        P(),
        P(None, ("tm", "wafer"), None),
        P(),
        P(("tm", "wafer"), None, None, None),
        P(("tm", "wafer"), None),
        P(),
        P("tm", None, None),
        P("tm", None, None),
        P(),
    )
    out_specs = (P("tm", None, None), P("tm", None, None), P("tm", None, None))
    return jax.shard_map(shards, mesh=mesh, in_specs=in_specs, out_specs=out_specs, check_vma=False)
```
